256 devices in a mesh: dp: 32 (over z, x_hi, core), ctx: 8 (over x_lo, y).
Axes of the slice: x: 4 (x_hi: 2, x_lo: 2; x = x_hi * 2 + x_lo), y: 4, z: 8, core: 2. Of those that a mesh axis runs over, the one named last changes fastest.
Arguments:
- query: bfloat16 [32, 1024, 1024], P('dp', 'ctx'), may hold values from -5 to 5
- key: bfloat16 [32, 1024, 512], P('dp', 'ctx'), may hold values from -5 to 5
- value: bfloat16 [32, 1024, 512], P('dp', 'ctx'), may hold values from -12 to 12
- out_weight: bfloat16 [1024, 2304], P('dp')
- post_gain: float32 [2304], replicated, may hold values from 0.25 to 4
- grad_out: bfloat16 [32, 1024, 2304], P('dp', 'ctx'), may hold values from -6 to 6
- block_lists: int32 [32, 8, 3], P('dp', 'ctx'), may hold values from -1 to 6, as said below
Outputs:
- grad_query: bfloat16 [32, 1024, 1024], P('dp', 'ctx')
- grad_key: bfloat16 [32, 1024, 512], P('dp', 'ctx')
- grad_value: bfloat16 [32, 1024, 512], P('dp', 'ctx')
- grad_wo: float32 [1024, 2304], P('dp')
- grad_gain: float32 [2304], replicated
The draws below stay inside these ranges and needn't reach their ends.
Inputs may be any that keep to these rules, and one draw needn't show every extreme that they name: `block_lists`: row b of each sequence holds, in its first min(3, b) slots, different block numbers below b, one of which is b - 1 when b >= 1, and -1 in its other slots.
All inputs are finite; a program needn't handle non-finite values.
Results may differ from the reference program's by a relative error of at most 0.02.
Values may be sent and summed in bfloat16 or wider, within the bound.
No kernel may reach another device: no remote copies, remote signals or barrier semaphores. Data moves between devices by JAX's collectives and lax.ppermute only.
A program may use at most 64 MiB of HBM per device.

```python
import math
import jax
import jax.numpy as jnp
from jax import lax

D = 2304
HD = 256
HQ = 4
HK = 2
BLK = 128
TOPK = 3
LEN = 1024
NBLK = 8
SEQS = 32


def drawn_pair(key):
    query_key = jax.random.fold_in(key, 101)
    key_key = jax.random.fold_in(key, 102)
    query_base = jnp.clip(jax.random.normal(query_key, (SEQS, LEN, HQ * HD), jnp.float32), -4.0, 4.0)
    key_base = jnp.clip(jax.random.normal(key_key, (SEQS, LEN, HK * HD), jnp.float32), -4.0, 4.0)
    return (query_base, key_base)


def draw_query(key, part):
    return drawn_pair(key)[0].astype(jnp.bfloat16)


def draw_key(key, part):
    return drawn_pair(key)[1].astype(jnp.bfloat16)


def draw_value(key, part):
    base_key = jax.random.fold_in(key, 201)
    scale_key = jax.random.fold_in(key, 202)
    base = jnp.clip(jax.random.normal(base_key, (SEQS, LEN, HK * HD), jnp.float32), -4.0, 4.0)
    row_scale = jnp.exp(jax.random.uniform(scale_key, (SEQS, LEN, 1), jnp.float32, -1.2, 1.0986))
    return (base * row_scale).astype(jnp.bfloat16)


def draw_out_weight(key, part):
    base_key = jax.random.fold_in(key, 301)
    scale_key = jax.random.fold_in(key, 302)
    fan_factor = float(HQ * HD) ** (-0.5)
    base = jnp.clip(jax.random.normal(base_key, (HQ * HD, D), jnp.float32), -4.0, 4.0)
    column_scale = jnp.exp(jax.random.uniform(scale_key, (1, D), jnp.float32, -1.2, 1.0986))
    return (base * column_scale * fan_factor).astype(jnp.bfloat16)


def draw_block_lists(key, part):
    scores = jax.random.randint(jax.random.fold_in(key, 401), (SEQS, NBLK, NBLK), 0, 1048576)
    columns = jnp.arange(NBLK, dtype=jnp.int32)
    distinct = scores * NBLK + columns[None, None, :]
    previous = columns[None, :] == columns[:, None] - 1
    distinct = jnp.where(previous[None, :, :], 1048576 * NBLK + NBLK, distinct)
    earlier = columns[None, :] < columns[:, None]
    ranked = jnp.where(earlier[None, :, :], distinct, -1)
    best, picked = lax.top_k(ranked, TOPK)
    return jnp.where(best >= 0, picked, -1).astype(jnp.int32)


def levels(stream_key, dims, split, least, top_value):
    loudness, own = 1.0, jax.random.fold_in(stream_key, 6)
    for axis_at, blocks in split:
        draws = jnp.exp(jax.random.uniform(jax.random.fold_in(own, axis_at), (blocks,), jnp.float32, least / len(split), top_value / len(split)))
        loudness = loudness * jnp.repeat(draws, dims[axis_at] // blocks).reshape([-1 if axis == axis_at else 1 for axis in range(len(dims))])
    return loudness


def gaussian(rng, dims, spread, limit, shards=(), held_as=jnp.bfloat16):
    entries = spread * jax.random.normal(rng, dims, jnp.float32)
    if shards:
        entries = entries * levels(rng, dims, shards, -0.22, 0.18)
    return jnp.clip(entries, -limit, limit).astype(held_as)


def setup_inputs(seed: int = 0) -> dict:
    key_list = jax.random.split(jax.random.key(seed), 8)
    return {
        "query": draw_query(jax.random.fold_in(key_list[7], 71), 0),
        "key": draw_key(jax.random.fold_in(key_list[7], 71), 0),
        "value": draw_value(jax.random.fold_in(key_list[7], 71), 0),
        "out_weight": draw_out_weight(jax.random.fold_in(key_list[7], 71), 0),
        "post_gain": jnp.clip(jnp.exp(jax.random.uniform(key_list[4], (D,), jnp.float32, math.log(0.25), math.log(4.0))), 0.25, 4.0),
        "grad_out": gaussian(key_list[5], (SEQS, LEN, D), 1.0, 6.0, ((0, 32), (1, 8))),
        "block_lists": draw_block_lists(jax.random.fold_in(key_list[7], 71), 0),
    }


SCALE = 0.0625
NEGATIVE = -1e+30
EPSILON = 1e-06

def to_low(values_in):
    return lax.optimization_barrier(values_in.astype(jnp.bfloat16))

def one_sequence(query_seq, key_seq, value_seq, grad_seq, block_ids, out_weight, post_gain):
    groups = HQ // HK
    positions = jnp.arange(LEN, dtype=jnp.int32)
    blocks = positions // BLK
    numbers = jnp.arange(NBLK, dtype=jnp.int32)
    chosen = jnp.any(block_ids[:, :, None] == numbers[None, None, :], axis=1)
    chosen = jnp.broadcast_to(chosen[:, None, :, None], (NBLK, BLK, NBLK, BLK)).reshape(LEN, LEN)
    own_block = (blocks[:, None] == blocks[None, :]) & (positions[None, :] <= positions[:, None])
    allowed = chosen | own_block
    queries = query_seq.astype(jnp.float32).reshape(LEN, HK, groups, HD)
    key_heads = key_seq.astype(jnp.float32).reshape(LEN, HK, HD)
    value_heads = value_seq.astype(jnp.float32).reshape(LEN, HK, HD)
    logits = jnp.einsum('tkgd,skd->kgts', queries, key_heads) * SCALE
    logits = jnp.where(allowed, logits, NEGATIVE)
    row_max = lax.optimization_barrier(jnp.max(logits, axis=-1))
    exp_total = lax.optimization_barrier(jnp.sum(jnp.where(allowed, jnp.exp(logits - row_max[..., None]), 0.0), axis=-1))
    log_total = row_max + jnp.log(exp_total)
    attn_probs = jnp.where(allowed, jnp.exp(logits - log_total[..., None]), 0.0)
    probs_low = to_low(attn_probs).astype(jnp.float32)
    heads_out = to_low(jnp.einsum('kgts,skd->tkgd', probs_low, value_heads)).reshape(LEN, HQ * HD)
    mixed_out = jnp.dot(heads_out, out_weight, preferred_element_type=jnp.float32)
    inv_rms = lax.rsqrt(lax.optimization_barrier(jnp.mean(mixed_out * mixed_out, axis=-1, keepdims=True)) + EPSILON)
    upstream = grad_seq.astype(jnp.float32)
    scaled = upstream * post_gain
    gain_term = lax.optimization_barrier(jnp.sum(upstream * mixed_out * inv_rms, axis=0))
    grad_mixed = to_low(inv_rms * (scaled - mixed_out * inv_rms * inv_rms * lax.optimization_barrier(jnp.mean(scaled * mixed_out, axis=-1, keepdims=True))))
    wo_term = jnp.dot(heads_out.T, grad_mixed, preferred_element_type=jnp.float32)
    grad_heads = to_low(jnp.dot(grad_mixed, out_weight.T, preferred_element_type=jnp.float32))
    grad_float = grad_heads.astype(jnp.float32).reshape(LEN, HK, groups, HD)
    heads_float = heads_out.astype(jnp.float32).reshape(LEN, HK, groups, HD)
    delta = jnp.einsum('tkgd,tkgd->kgt', grad_float, heads_float)
    grad_probs = jnp.einsum('tkgd,skd->kgts', grad_float, value_heads)
    grad_logits = to_low(jnp.where(allowed, attn_probs * (grad_probs - delta[..., None]) * SCALE, 0.0)).astype(jnp.float32)
    grad_query = jnp.einsum('kgts,skd->tkgd', grad_logits, key_heads).astype(jnp.bfloat16).reshape(LEN, HQ * HD)
    grad_key = jnp.einsum('kgts,tkgd->skd', grad_logits, queries).astype(jnp.bfloat16).reshape(LEN, HK * HD)
    grad_value = jnp.einsum('kgts,tkgd->skd', probs_low, grad_float).astype(jnp.bfloat16).reshape(LEN, HK * HD)
    return (grad_query, grad_key, grad_value, wo_term, gain_term)

def reference(query, key, value, out_weight, post_gain, grad_out, block_lists):

    def per_sequence(carried, inputs):
        wo_total, gain_total = carried
        query_seq, key_seq, value_seq, grad_seq, block_ids = inputs
        results = one_sequence(query_seq, key_seq, value_seq, grad_seq, block_ids, out_weight, post_gain)
        return ((wo_total + results[3], gain_total + results[4]), (results[0], results[1], results[2]))
    start_state = (jnp.zeros((HQ * HD, D), jnp.float32), jnp.zeros((D,), jnp.float32))
    sums, grads = lax.scan(per_sequence, start_state, (query, key, value, grad_out, block_lists))
    return (grads[0], grads[1], grads[2], sums[0] / SEQS, sums[1] / SEQS)
```

```python
import jax
import jax.numpy as jnp
from jax import lax
from jax.sharding import PartitionSpec as P

HD = 256
HQ = 4
HK = 2
BLK = 128
TOPK = 3


SCALE = 0.0625
NEGATIVE = -1e30
EPSILON = 1e-06

DP_REDUCE_MASKS = (1, 4, 2, 8, 16)


def xor_pairs(size, mask):
    return [(i, i ^ mask) for i in range(size)]


def bit_of(axis, mask):
    return (lax.axis_index(axis) // mask) % 2


def gather_xor(block, axis, size, masks):
    bits = size.bit_length() - 1
    done = []
    held = block
    for mask in [m for m in masks if m < size]:
        theirs = lax.ppermute(held, axis, xor_pairs(size, mask))
        mine_high = bit_of(axis, mask) == 1
        low = jnp.where(mine_high, theirs, held)
        high = jnp.where(mine_high, held, theirs)
        pos = sum(1 for m in done if m > mask)
        held = jnp.stack([low, high], axis=pos)
        done.append(mask)
    assert len(done) == bits
    return held.reshape((size * block.shape[0],) + block.shape[1:])


def reduce_scatter_xor(full, axis, size, masks, send_dtype):
    bits = size.bit_length() - 1
    rows = full.shape[0] // size
    held = full.reshape((2,) * bits + (rows,) + full.shape[1:])
    left = [1 << (bits - 1 - i) for i in range(bits)]
    for mask in [m for m in masks if m < size]:
        pos = left.index(mask)
        mine = bit_of(axis, mask)
        keep = lax.dynamic_index_in_dim(held, mine, axis=pos, keepdims=False)
        send = lax.dynamic_index_in_dim(held, 1 - mine, axis=pos, keepdims=False)
        theirs = lax.ppermute(send.astype(send_dtype), axis, xor_pairs(size, mask))
        held = keep.astype(jnp.float32) + theirs.astype(jnp.float32)
        left.remove(mask)
    return held


def all_reduce_xor(value, axis, size):
    mask = 1
    while mask < size:
        value = value + lax.ppermute(value, axis, xor_pairs(size, mask))
        mask *= 2
    return value


def per_device(query, key, value, out_weight, post_gain, grad_out, block_lists):
    tokens = query.shape[1]
    assert tokens == BLK
    groups = HQ // HK
    n_ctx = lax.axis_size("ctx")
    n_dp = lax.axis_size("dp")
    ctx_rank = lax.axis_index("ctx")
    kv_width = key.shape[2]

    own_kv = jnp.concatenate([key[0], value[0]], axis=-1)
    kv_parts = [own_kv]
    for s in range(1, n_ctx):
        kv_parts.append(lax.ppermute(own_kv, "ctx", [(i, i + s) for i in range(n_ctx - s)]))
    kv_all = jnp.stack(kv_parts)
    key_rows = kv_all[..., :kv_width].reshape(n_ctx * BLK, HK, HD)
    value_rows = kv_all[..., kv_width:].reshape(n_ctx * BLK, HK, HD)

    block_ids = block_lists[0, 0]
    shifts = lax.iota(jnp.int32, n_ctx)
    source = ctx_rank - shifts
    chosen = (source >= 0) & jnp.any(block_ids[None, :] == source[:, None], axis=1)
    inner = lax.iota(jnp.int32, BLK)
    causal = inner[None, :] <= inner[:, None]
    allowed = jnp.where(
        (shifts == 0)[:, None, None], causal[None], chosen[:, None, None]
    )
    allowed = jnp.transpose(allowed, (1, 0, 2)).reshape(BLK, n_ctx * BLK)

    weight_full = gather_xor(out_weight, "dp", n_dp, DP_REDUCE_MASKS[::-1])

    queries = query[0].reshape(BLK, HK, groups, HD)
    raw = jnp.einsum("tkgd,ukd->kgtu", queries, key_rows, preferred_element_type=jnp.float32)
    logits = jnp.where(allowed, raw * SCALE, NEGATIVE)
    row_max = jnp.max(logits, axis=-1)
    exp_total = jnp.sum(jnp.where(allowed, jnp.exp(logits - row_max[..., None]), 0.0), axis=-1)
    log_total = row_max + jnp.log(exp_total)
    attn_probs = jnp.where(allowed, jnp.exp(logits - log_total[..., None]), 0.0)
    probs_low = attn_probs.astype(jnp.bfloat16)
    heads_out = jnp.einsum(
        "kgtu,ukd->tkgd", probs_low, value_rows, preferred_element_type=jnp.float32
    ).astype(jnp.bfloat16)
    heads_flat = heads_out.reshape(tokens, HQ * HD)

    mixed_out = jnp.dot(heads_flat, weight_full, preferred_element_type=jnp.float32)
    inv_rms = lax.rsqrt(jnp.mean(mixed_out * mixed_out, axis=-1, keepdims=True) + EPSILON)
    upstream = grad_out[0].astype(jnp.float32)
    scaled = upstream * post_gain
    gain_term = jnp.sum(upstream * mixed_out * inv_rms, axis=0)
    grad_mixed = (
        inv_rms
        * (
            scaled
            - mixed_out * inv_rms * inv_rms * jnp.mean(scaled * mixed_out, axis=-1, keepdims=True)
        )
    ).astype(jnp.bfloat16)

    wo_term = lax.dot_general(
        heads_flat, grad_mixed, (((0,), (0,)), ((), ())), preferred_element_type=jnp.float32
    )
    wo_block = reduce_scatter_xor(wo_term, "dp", n_dp, DP_REDUCE_MASKS, jnp.bfloat16)
    wo_sum = all_reduce_xor(wo_block, "ctx", n_ctx)
    gain_sum = all_reduce_xor(all_reduce_xor(gain_term, "ctx", n_ctx), "dp", n_dp)

    grad_heads = lax.dot_general(
        grad_mixed, weight_full, (((1,), (1,)), ((), ())), preferred_element_type=jnp.float32
    ).astype(jnp.bfloat16)
    grad_float = grad_heads.reshape(BLK, HK, groups, HD)
    delta = jnp.einsum(
        "tkgd,tkgd->kgt", grad_float, heads_out, preferred_element_type=jnp.float32
    )
    grad_probs = jnp.einsum(
        "tkgd,ukd->kgtu", grad_float, value_rows, preferred_element_type=jnp.float32
    )
    grad_logits = jnp.where(
        allowed, attn_probs * (grad_probs - delta[..., None]) * SCALE, 0.0
    ).astype(jnp.bfloat16)
    grad_query = jnp.einsum(
        "kgtu,ukd->tkgd", grad_logits, key_rows, preferred_element_type=jnp.float32
    ).astype(jnp.bfloat16)
    key_part = jnp.einsum(
        "kgtu,tkgd->ukd", grad_logits, queries, preferred_element_type=jnp.float32
    )
    value_part = jnp.einsum(
        "kgtu,tkgd->ukd", probs_low, grad_float, preferred_element_type=jnp.float32
    )
    kv_grad = jnp.concatenate(
        [key_part.reshape(n_ctx, BLK, kv_width), value_part.reshape(n_ctx, BLK, kv_width)],
        axis=-1,
    )
    total = kv_grad[0]
    for s in range(1, n_ctx):
        back = lax.ppermute(
            kv_grad[s].astype(jnp.bfloat16), "ctx", [(i, i - s) for i in range(s, n_ctx)]
        )
        total = total + back.astype(jnp.float32)

    seq_count = float(n_dp)
    grad_query_out = grad_query.reshape(1, tokens, HQ * HD)
    grad_key_out = total[:, :kv_width].astype(jnp.bfloat16).reshape(1, tokens, kv_width)
    grad_value_out = total[:, kv_width:].astype(jnp.bfloat16).reshape(1, tokens, kv_width)
    return (grad_query_out, grad_key_out, grad_value_out, wo_sum / seq_count, gain_sum / seq_count)


def solution(mesh):
    in_specs = (
        P("dp", "ctx", None),
        P("dp", "ctx", None),
        P("dp", "ctx", None),
        P("dp", None),
        P(),
        P("dp", "ctx", None),
        P("dp", "ctx", None),
    )
    out_specs = (
        P("dp", "ctx", None),
        P("dp", "ctx", None),
        P("dp", "ctx", None),
        P("dp", None),
        P(),
    )
    return jax.shard_map(
        per_device, mesh=mesh, in_specs=in_specs, out_specs=out_specs, check_vma=False
    )
```

```python
import jax
import jax.numpy as jnp
from jax import lax
from jax.sharding import PartitionSpec as P

HD = 256
HQ = 4
HK = 2
BLK = 128
TOPK = 3


SCALE = 0.0625
NEGATIVE = -1e30
EPSILON = 1e-06


def xor_pairs(size, mask0, mask1=None):
    mask1 = mask0 if mask1 is None else mask1
    return [(i, i ^ (mask0 if i % 2 == 0 else mask1)) for i in range(size)]


def bit_of(axis, mask):
    return (lax.axis_index(axis) // mask) % 2


def core_bit(axis):
    return lax.axis_index(axis) % 2


def own_bit(axis, mask0, mask1):
    mask = jnp.where(core_bit(axis) == 0, mask0, mask1)
    return (lax.axis_index(axis) // mask) % 2


def split_rounds(size):
    bits = size.bit_length() - 1
    high = [1 << k for k in range(3, bits)]
    return [(1, 1), (4, 2), (2, 4)] + [(m, m) for m in high]


def gather_dp(block, axis, size):
    rounds = split_rounds(size)[::-1]
    held = block
    count = 0
    for mask0, mask1 in rounds:
        theirs = lax.ppermute(held, axis, xor_pairs(size, mask0, mask1))
        mine_high = own_bit(axis, mask0, mask1) == 1
        if mask0 == 1:
            held = jnp.where(core_bit(axis) == 0, jnp.swapaxes(held, count - 2, count - 1), held)
            theirs = jnp.where(core_bit(axis) == 0, theirs, jnp.swapaxes(theirs, count - 2, count - 1))
        low = jnp.where(mine_high, theirs, held)
        high = jnp.where(mine_high, held, theirs)
        held = jnp.stack([low, high], axis=count)
        count += 1
    return held.reshape((size * block.shape[0],) + block.shape[1:])


def split_hi_lo(value):
    hi = value.astype(jnp.bfloat16)
    lo = (value - hi.astype(jnp.float32)).astype(jnp.bfloat16)
    return hi, lo


def reduce_scatter_dp(full, gain, axis, size):
    bits = size.bit_length() - 1
    rows = full.shape[0] // size
    cols = full.shape[1]
    held = full.reshape((2,) * bits + (rows, cols))
    for mask0, mask1 in split_rounds(size):
        pos = held.ndim - 3
        if mask0 == 4:
            held = jnp.where(core_bit(axis) == 1, jnp.swapaxes(held, pos - 1, pos), held)
            pos = pos - 1
        mine = own_bit(axis, mask0, mask1)
        keep = lax.dynamic_index_in_dim(held, mine, axis=pos, keepdims=False)
        send = lax.dynamic_index_in_dim(held, 1 - mine, axis=pos, keepdims=False)
        hi, lo = split_hi_lo(gain)
        packet = jnp.concatenate(
            [send.astype(jnp.bfloat16).reshape(-1, cols), hi[None], lo[None]], axis=0
        )
        theirs = lax.ppermute(packet, axis, xor_pairs(size, mask0, mask1))
        got = theirs[:-2].reshape(send.shape).astype(jnp.float32)
        held = keep.astype(jnp.float32) + got
        mine_gain = hi.astype(jnp.float32) + lo.astype(jnp.float32)
        their_gain = theirs[-2].astype(jnp.float32) + theirs[-1].astype(jnp.float32)
        gain = mine_gain + their_gain
    return held.reshape(rows, cols), gain


def all_reduce_xor(value, axis, size):
    mask = 1
    while mask < size:
        value = value + lax.ppermute(value, axis, xor_pairs(size, mask))
        mask *= 2
    return value


def per_device(query, key, value, out_weight, post_gain, grad_out, block_lists):
    tokens = query.shape[1]
    assert tokens == BLK
    groups = HQ // HK
    n_ctx = lax.axis_size("ctx")
    n_dp = lax.axis_size("dp")
    ctx_rank = lax.axis_index("ctx")
    kv_width = key.shape[2]

    own_kv = jnp.concatenate([key[0], value[0]], axis=-1)
    kv_parts = [own_kv]
    for s in range(1, n_ctx):
        kv_parts.append(lax.ppermute(own_kv, "ctx", [(i, i + s) for i in range(n_ctx - s)]))
    kv_all = jnp.stack(kv_parts)
    key_rows = kv_all[..., :kv_width].reshape(n_ctx * BLK, HK, HD)
    value_rows = kv_all[..., kv_width:].reshape(n_ctx * BLK, HK, HD)

    block_ids = block_lists[0, 0]
    shifts = lax.iota(jnp.int32, n_ctx)
    source = ctx_rank - shifts
    chosen = (source >= 0) & jnp.any(block_ids[None, :] == source[:, None], axis=1)
    inner = lax.iota(jnp.int32, BLK)
    causal = inner[None, :] <= inner[:, None]
    allowed = jnp.where(
        (shifts == 0)[:, None, None], causal[None], chosen[:, None, None]
    )
    allowed = jnp.transpose(allowed, (1, 0, 2)).reshape(BLK, n_ctx * BLK)

    weight_full = gather_dp(out_weight, "dp", n_dp)

    queries = query[0].reshape(BLK, HK, groups, HD)
    raw = jnp.einsum("tkgd,ukd->kgtu", queries, key_rows, preferred_element_type=jnp.float32)
    logits = jnp.where(allowed, raw * SCALE, NEGATIVE)
    row_max = jnp.max(logits, axis=-1)
    exp_total = jnp.sum(jnp.where(allowed, jnp.exp(logits - row_max[..., None]), 0.0), axis=-1)
    log_total = row_max + jnp.log(exp_total)
    attn_probs = jnp.where(allowed, jnp.exp(logits - log_total[..., None]), 0.0)
    probs_low = attn_probs.astype(jnp.bfloat16)
    heads_out = jnp.einsum(
        "kgtu,ukd->tkgd", probs_low, value_rows, preferred_element_type=jnp.float32
    ).astype(jnp.bfloat16)
    heads_flat = heads_out.reshape(tokens, HQ * HD)

    mixed_out = jnp.dot(heads_flat, weight_full, preferred_element_type=jnp.float32)
    inv_rms = lax.rsqrt(jnp.mean(mixed_out * mixed_out, axis=-1, keepdims=True) + EPSILON)
    upstream = grad_out[0].astype(jnp.float32)
    scaled = upstream * post_gain
    gain_term = jnp.sum(upstream * mixed_out * inv_rms, axis=0)
    grad_mixed = (
        inv_rms
        * (
            scaled
            - mixed_out * inv_rms * inv_rms * jnp.mean(scaled * mixed_out, axis=-1, keepdims=True)
        )
    ).astype(jnp.bfloat16)

    wo_term = lax.dot_general(
        heads_flat, grad_mixed, (((0,), (0,)), ((), ())), preferred_element_type=jnp.float32
    )
    wo_block, gain_dp = reduce_scatter_dp(wo_term, gain_term, "dp", n_dp)
    sums = all_reduce_xor(jnp.concatenate([wo_block, gain_dp[None]], axis=0), "ctx", n_ctx)
    wo_sum = sums[:-1]
    gain_sum = sums[-1]

    grad_heads = lax.dot_general(
        grad_mixed, weight_full, (((1,), (1,)), ((), ())), preferred_element_type=jnp.float32
    ).astype(jnp.bfloat16)
    grad_float = grad_heads.reshape(BLK, HK, groups, HD)
    delta = jnp.einsum(
        "tkgd,tkgd->kgt", grad_float, heads_out, preferred_element_type=jnp.float32
    )
    grad_probs = jnp.einsum(
        "tkgd,ukd->kgtu", grad_float, value_rows, preferred_element_type=jnp.float32
    )
    grad_logits = jnp.where(
        allowed, attn_probs * (grad_probs - delta[..., None]) * SCALE, 0.0
    ).astype(jnp.bfloat16)
    grad_query = jnp.einsum(
        "kgtu,ukd->tkgd", grad_logits, key_rows, preferred_element_type=jnp.float32
    ).astype(jnp.bfloat16)
    key_part = jnp.einsum(
        "kgtu,tkgd->ukd", grad_logits, queries, preferred_element_type=jnp.float32
    )
    value_part = jnp.einsum(
        "kgtu,tkgd->ukd", probs_low, grad_float, preferred_element_type=jnp.float32
    )
    kv_grad = jnp.concatenate(
        [key_part.reshape(n_ctx, BLK, kv_width), value_part.reshape(n_ctx, BLK, kv_width)],
        axis=-1,
    )
    total = kv_grad[0]
    for s in range(1, n_ctx):
        back = lax.ppermute(
            kv_grad[s].astype(jnp.bfloat16), "ctx", [(i, i - s) for i in range(s, n_ctx)]
        )
        total = total + back.astype(jnp.float32)

    seq_count = float(n_dp)
    grad_query_out = grad_query.reshape(1, tokens, HQ * HD)
    grad_key_out = total[:, :kv_width].astype(jnp.bfloat16).reshape(1, tokens, kv_width)
    grad_value_out = total[:, kv_width:].astype(jnp.bfloat16).reshape(1, tokens, kv_width)
    return (grad_query_out, grad_key_out, grad_value_out, wo_sum / seq_count, gain_sum / seq_count)


def solution(mesh):
    in_specs = (
        P("dp", "ctx", None),
        P("dp", "ctx", None),
        P("dp", "ctx", None),
        P("dp", None),
        P(),
        P("dp", "ctx", None),
        P("dp", "ctx", None),
    )
    out_specs = (
        P("dp", "ctx", None),
        P("dp", "ctx", None),
        P("dp", "ctx", None),
        P("dp", None),
        P(),
    )
    return jax.shard_map(
        per_device, mesh=mesh, in_specs=in_specs, out_specs=out_specs, check_vma=False
    )
```

```python
import jax
import jax.numpy as jnp
from jax import lax
from jax.sharding import PartitionSpec as P


HD = 256
HQ = 4
HK = 2
BLK = 128


SCALE = 0.0625
NEGATIVE = -1e30
EPSILON = 1e-06


def xor_pairs(size, mask0, mask1=None):
    mask1 = mask0 if mask1 is None else mask1
    return [(i, i ^ (mask0 if i % 2 == 0 else mask1)) for i in range(size)]


def core_bit(axis):
    return lax.axis_index(axis) % 2


def z_shift(size):
    return 2 if size // 4 >= 4 else 0


def dp_label(index, size):
    if index % 2 == 0:
        return index
    z, rest = divmod(index, 4)
    return ((z + z_shift(size)) % (size // 4)) * 4 + rest


def dp_unlabel(label, size):
    if label % 2 == 0:
        return label
    z, rest = divmod(label, 4)
    return ((z - z_shift(size)) % (size // 4)) * 4 + rest


def dp_pairs(size, mask0, mask1):
    if mask0 == 1:
        return [(i, i ^ 1) for i in range(size)]
    pairs = []
    for i in range(size):
        mask = mask0 if i % 2 == 0 else mask1
        pairs.append((i, dp_unlabel(dp_label(i, size) ^ mask, size)))
    return pairs


def own_bit(axis, size, mask0, mask1):
    index = lax.axis_index(axis)
    if mask0 != 1:
        shifted = ((index // 4 + z_shift(size)) % (size // 4)) * 4 + index % 4
        index = jnp.where(index % 2 == 1, shifted, index)
    mask = jnp.where(core_bit(axis) == 0, mask0, mask1)
    return (index // mask) % 2


def roll_z(held, size, amount):
    lead = held.ndim - 2 - 1
    shape = held.shape
    zs = size // 4
    grouped = held.reshape((zs,) + shape[lead:])
    return jnp.roll(grouped, amount, axis=0).reshape(shape)


def split_rounds(size):
    bits = size.bit_length() - 1
    high = [1 << k for k in range(3, bits)]
    return [(1, 1), (4, 2), (2, 4)] + [(m, m) for m in high]


def gather_dp(block, axis, size):
    rounds = split_rounds(size)[::-1]
    held = block
    count = 0
    for mask0, mask1 in rounds:
        if mask0 == 1:
            held = jnp.where(
                core_bit(axis) == 0,
                jnp.swapaxes(held, count - 2, count - 1),
                roll_z(held, size, -z_shift(size)),
            )
        theirs = lax.ppermute(held, axis, dp_pairs(size, mask0, mask1))
        mine_high = own_bit(axis, size, mask0, mask1) == 1
        low = jnp.where(mine_high, theirs, held)
        high = jnp.where(mine_high, held, theirs)
        held = jnp.stack([low, high], axis=count)
        count += 1
    return held.reshape((size * block.shape[0],) + block.shape[1:])


def wo_order(size):
    order = []
    for q in range(size):
        if q % 2 == 0:
            order.append(q)
            continue
        high, x_hi, z_low = q >> 3, (q >> 2) & 1, (q >> 1) & 1
        z = (high * 2 + z_low - z_shift(size)) % (size // 4)
        order.append(z * 4 + x_hi * 2 + 1)
    return order


def split_hi_lo(value):
    hi = value.astype(jnp.bfloat16)
    lo = (value - hi.astype(jnp.float32)).astype(jnp.bfloat16)
    return hi, lo


def reduce_scatter_dp(full, gain, axis, size):
    bits = size.bit_length() - 1
    rows = full.shape[0] // size
    cols = full.shape[1]
    held = full.reshape((2,) * bits + (rows, cols))
    for mask0, mask1 in split_rounds(size):
      pos = held.ndim - 3
      if mask0 == 4:
          pos = pos - 1
      mine = own_bit(axis, size, mask0, mask1)
      keep = lax.dynamic_index_in_dim(held, mine, axis=pos, keepdims=False)
      send = lax.dynamic_index_in_dim(held, 1 - mine, axis=pos, keepdims=False)
      hi, lo = split_hi_lo(gain)
      packet = jnp.concatenate(
          [send.astype(jnp.bfloat16).reshape(-1, cols), hi[None], lo[None]], axis=0
      )
      theirs = lax.ppermute(packet, axis, dp_pairs(size, mask0, mask1))
      got = theirs[:-2].reshape(send.shape).astype(jnp.float32)
      held = keep.astype(jnp.float32) + got
      mine_gain = hi.astype(jnp.float32) + lo.astype(jnp.float32)
      their_gain = theirs[-2].astype(jnp.float32) + theirs[-1].astype(jnp.float32)
      gain = mine_gain + their_gain
    return held.reshape(rows, cols), gain


def all_reduce_ctx(value, n_dp, n_ctx):
    bits = n_ctx.bit_length() - 1
    order0 = [1 << k for k in range(bits)]
    order1 = order0[-1:] + order0[:-1]
    for mask0, mask1 in zip(order0, order1):
        perm = []
        for d in range(n_dp):
            mask = mask0 if d % 2 == 0 else mask1
            perm += [(d * n_ctx + c, d * n_ctx + (c ^ mask)) for c in range(n_ctx)]
        value = value + lax.ppermute(value, ("dp", "ctx"), perm)
    return value


def gather_ctx(block, size):
    held = block
    done = []
    for mask in (2, 1, 4):
        if mask >= size:
            continue
        theirs = lax.ppermute(held, "ctx", xor_pairs(size, mask))
        pos = sum(1 for m in done if m > mask)
        held = jnp.stack([held, theirs], axis=pos)
        done.append(mask)
    return held.reshape((size * block.shape[0],) + block.shape[1:])


def per_device(query, key, value, out_weight, post_gain, grad_out, block_lists):
    tokens = query.shape[1]
    assert tokens == BLK
    groups = HQ // HK
    n_ctx = lax.axis_size("ctx")
    n_dp = lax.axis_size("dp")
    ctx_rank = lax.axis_index("ctx")
    kv_width = key.shape[2]

    own_kv = jnp.concatenate([key[0], value[0]], axis=-1)
    kv_all = gather_ctx(own_kv, n_ctx)
    key_rows = kv_all[:, :kv_width].reshape(n_ctx * BLK, HK, HD)
    value_rows = kv_all[:, kv_width:].reshape(n_ctx * BLK, HK, HD)

    block_ids = block_lists[0, 0]
    offsets = lax.iota(jnp.int32, n_ctx)
    numbers = jnp.bitwise_xor(ctx_rank, offsets)
    chosen = jnp.any(block_ids[None, :] == numbers[:, None], axis=1)
    inner = lax.iota(jnp.int32, BLK)
    causal = inner[None, :] <= inner[:, None]
    allowed = jnp.where(
        (offsets == 0)[:, None, None], causal[None], chosen[:, None, None]
    )
    allowed = jnp.transpose(allowed, (1, 0, 2)).reshape(BLK, n_ctx * BLK)

    weight_full = gather_dp(out_weight, "dp", n_dp)

    queries = query[0].reshape(BLK, HK, groups, HD)
    raw = jnp.einsum("tkgd,ukd->kgtu", queries, key_rows, preferred_element_type=jnp.float32)
    logits = jnp.where(allowed, raw * SCALE, NEGATIVE)
    row_max = jnp.max(logits, axis=-1)
    exp_total = jnp.sum(jnp.where(allowed, jnp.exp(logits - row_max[..., None]), 0.0), axis=-1)
    log_total = row_max + jnp.log(exp_total)
    attn_probs = jnp.where(allowed, jnp.exp(logits - log_total[..., None]), 0.0)
    probs_low = attn_probs.astype(jnp.bfloat16)
    heads_out = jnp.einsum(
        "kgtu,ukd->tkgd", probs_low, value_rows, preferred_element_type=jnp.float32
    ).astype(jnp.bfloat16)
    heads_flat = heads_out.reshape(tokens, HQ * HD)

    mixed_out = jnp.dot(heads_flat, weight_full, preferred_element_type=jnp.float32)
    inv_rms = lax.rsqrt(jnp.mean(mixed_out * mixed_out, axis=-1, keepdims=True) + EPSILON)
    upstream = grad_out[0].astype(jnp.float32)
    scaled = upstream * post_gain
    gain_term = jnp.sum(upstream * mixed_out * inv_rms, axis=0)
    grad_mixed = (
        inv_rms
        * (
            scaled
            - mixed_out * inv_rms * inv_rms * jnp.mean(scaled * mixed_out, axis=-1, keepdims=True)
        )
    ).astype(jnp.bfloat16)

    blocks_of_heads = heads_flat.reshape(tokens, n_dp, -1)
    heads_in_order = blocks_of_heads[:, jnp.array(wo_order(n_dp), jnp.int32), :]
    wo_term = lax.dot_general(
        heads_in_order.reshape(tokens, -1),
        grad_mixed,
        (((0,), (0,)), ((), ())),
        preferred_element_type=jnp.float32,
    )
    wo_block, gain_dp = reduce_scatter_dp(wo_term, gain_term, "dp", n_dp)
    sums = all_reduce_ctx(jnp.concatenate([wo_block, gain_dp[None]], axis=0), n_dp, n_ctx)
    wo_sum = sums[:-1]
    gain_sum = sums[-1]

    grad_heads = lax.dot_general(
        grad_mixed, weight_full, (((1,), (1,)), ((), ())), preferred_element_type=jnp.float32
    ).astype(jnp.bfloat16)
    grad_float = grad_heads.reshape(BLK, HK, groups, HD)
    delta = jnp.einsum(
        "tkgd,tkgd->kgt", grad_float, heads_out, preferred_element_type=jnp.float32
    )
    grad_probs = jnp.einsum(
        "tkgd,ukd->kgtu", grad_float, value_rows, preferred_element_type=jnp.float32
    )
    grad_logits = jnp.where(
        allowed, attn_probs * (grad_probs - delta[..., None]) * SCALE, 0.0
    ).astype(jnp.bfloat16)
    grad_query = jnp.einsum(
        "kgtu,ukd->tkgd", grad_logits, key_rows, preferred_element_type=jnp.float32
    ).astype(jnp.bfloat16)
    key_part = jnp.einsum(
        "kgtu,tkgd->ukd", grad_logits, queries, preferred_element_type=jnp.float32
    )
    value_part = jnp.einsum(
        "kgtu,tkgd->ukd", probs_low, grad_float, preferred_element_type=jnp.float32
    )
    kv_grad = jnp.concatenate(
        [key_part.reshape(n_ctx, BLK, kv_width), value_part.reshape(n_ctx, BLK, kv_width)],
        axis=-1,
    )
    total = kv_grad[0]
    for p in range(1, n_ctx):
        back = lax.ppermute(
            kv_grad[p].astype(jnp.bfloat16),
            "ctx",
            [(i, i ^ p) for i in range(n_ctx) if (i ^ p) < i],
        )
        total = total + back.astype(jnp.float32)

    seq_count = float(n_dp)
    grad_query_out = grad_query.reshape(1, tokens, HQ * HD)
    grad_key_out = total[:, :kv_width].astype(jnp.bfloat16).reshape(1, tokens, kv_width)
    grad_value_out = total[:, kv_width:].astype(jnp.bfloat16).reshape(1, tokens, kv_width)
    return (grad_query_out, grad_key_out, grad_value_out, wo_sum / seq_count, gain_sum / seq_count)


def solution(mesh):
    in_specs = (
        P("dp", "ctx", None),
        P("dp", "ctx", None),
        P("dp", "ctx", None),
        P("dp", None),
        P(),
        P("dp", "ctx", None),
        P("dp", "ctx", None),
    )
    out_specs = (
        P("dp", "ctx", None),
        P("dp", "ctx", None),
        P("dp", "ctx", None),
        P("dp", None),
        P(),
    )

    return jax.shard_map(
        per_device, mesh=mesh, in_specs=in_specs, out_specs=out_specs, check_vma=False
    )
```

```python
import jax
import jax.numpy as jnp
from jax import lax
from jax.sharding import PartitionSpec as P


HD = 256
HQ = 4
HK = 2
BLK = 128


SCALE = 0.0625
NEGATIVE = -1e30
EPSILON = 1e-06


def xor_pairs(size, mask0, mask1=None):
    mask1 = mask0 if mask1 is None else mask1
    return [(i, i ^ (mask0 if i % 2 == 0 else mask1)) for i in range(size)]


def bit_of(axis, mask):
    return (lax.axis_index(axis) // mask) % 2


def core_bit(axis):
    return lax.axis_index(axis) % 2


def z_shift(size):
    return 2 if size // 4 >= 4 else 0


def dp_label(index, size):
    if index % 2 == 0:
        return index
    z, rest = divmod(index, 4)
    return ((z + z_shift(size)) % (size // 4)) * 4 + rest


def dp_unlabel(label, size):
    if label % 2 == 0:
        return label
    z, rest = divmod(label, 4)
    return ((z - z_shift(size)) % (size // 4)) * 4 + rest


def dp_pairs(size, mask0, mask1):
    if mask0 == 1:
        return [(i, i ^ 1) for i in range(size)]
    pairs = []
    for i in range(size):
        mask = mask0 if i % 2 == 0 else mask1
        pairs.append((i, dp_unlabel(dp_label(i, size) ^ mask, size)))
    return pairs


def own_bit(axis, size, mask0, mask1):
    index = lax.axis_index(axis)
    if mask0 != 1:
        shifted = ((index // 4 + z_shift(size)) % (size // 4)) * 4 + index % 4
        index = jnp.where(index % 2 == 1, shifted, index)
    mask = jnp.where(core_bit(axis) == 0, mask0, mask1)
    return (index // mask) % 2


def split_rounds(size):
    bits = size.bit_length() - 1
    high = [1 << k for k in range(3, bits)]
    return [(1, 1), (4, 2), (2, 4)] + [(m, m) for m in high]


def gather_dp(block, axis, size):
    rounds = split_rounds(size)[::-1]
    held = block
    count = 0
    for mask0, mask1 in rounds:
        theirs = lax.ppermute(held, axis, dp_pairs(size, mask0, mask1))
        mine_high = own_bit(axis, size, mask0, mask1) == 1
        low = jnp.where(mine_high, theirs, held)
        high = jnp.where(mine_high, held, theirs)
        held = jnp.stack([low, high], axis=count)
        count += 1
    return held.reshape((size * block.shape[0],) + block.shape[1:])


def wo_order(size):
    order = []
    for q in range(size):
        if q % 2 == 0:
            order.append(q)
            continue
        high, x_hi, z_low = q >> 3, (q >> 2) & 1, (q >> 1) & 1
        z = (high * 2 + z_low - z_shift(size)) % (size // 4)
        order.append(z * 4 + x_hi * 2 + 1)
    return order


def w_order(size):
    order = []
    for q in range(size):
        high, upper, lower = q >> 3, (q >> 2) & 1, (q >> 1) & 1
        if q % 2 == 0:
            order.append((high * 2 + lower) * 4 + upper * 2)
        else:
            z = (high * 2 + upper - z_shift(size)) % (size // 4)
            order.append(z * 4 + lower * 2 + 1)
    return order


def split_hi_lo(value):
    hi = value.astype(jnp.bfloat16)
    lo = (value - hi.astype(jnp.float32)).astype(jnp.bfloat16)
    return hi, lo


def reduce_scatter_dp(full, gain, axis, size):
    bits = size.bit_length() - 1
    rows = full.shape[0] // size
    cols = full.shape[1]
    held = full.reshape((2,) * bits + (rows, cols))
    for mask0, mask1 in split_rounds(size):
      pos = held.ndim - 3
      if mask0 == 4:
          pos = pos - 1
      mine = own_bit(axis, size, mask0, mask1)
      keep = lax.dynamic_index_in_dim(held, mine, axis=pos, keepdims=False)
      send = lax.dynamic_index_in_dim(held, 1 - mine, axis=pos, keepdims=False)
      hi, lo = split_hi_lo(gain)
      packet = jnp.concatenate(
          [send.astype(jnp.bfloat16).reshape(-1, cols), hi[None], lo[None]], axis=0
      )
      theirs = lax.ppermute(packet, axis, dp_pairs(size, mask0, mask1))
      got = theirs[:-2].reshape(send.shape).astype(jnp.float32)
      held = keep.astype(jnp.float32) + got
      mine_gain = hi.astype(jnp.float32) + lo.astype(jnp.float32)
      their_gain = theirs[-2].astype(jnp.float32) + theirs[-1].astype(jnp.float32)
      gain = mine_gain + their_gain
    return held.reshape(rows, cols), gain


def all_reduce_ctx(value, n_dp, n_ctx):
    bits = n_ctx.bit_length() - 1
    order0 = [1 << k for k in range(bits)]
    order1 = order0[-1:] + order0[:-1]
    for mask0, mask1 in zip(order0, order1):
        perm = []
        for d in range(n_dp):
            mask = mask0 if d % 2 == 0 else mask1
            perm += [(d * n_ctx + c, d * n_ctx + (c ^ mask)) for c in range(n_ctx)]
        value = value + lax.ppermute(value, ("dp", "ctx"), perm)
    return value


def gather_ctx(block, size):
    held = block
    done = []
    for mask in (2, 1, 4):
        if mask >= size:
            continue
        theirs = lax.ppermute(held, "ctx", xor_pairs(size, mask))
        mine_high = bit_of("ctx", mask) == 1
        low = jnp.where(mine_high, theirs, held)
        high = jnp.where(mine_high, held, theirs)
        pos = sum(1 for m in done if m > mask)
        held = jnp.stack([low, high], axis=pos)
        done.append(mask)
    return held.reshape((size * block.shape[0],) + block.shape[1:])


def per_device(query, key, value, out_weight, post_gain, grad_out, block_lists):
    tokens = query.shape[1]
    assert tokens == BLK
    groups = HQ // HK
    n_ctx = lax.axis_size("ctx")
    n_dp = lax.axis_size("dp")
    ctx_rank = lax.axis_index("ctx")
    kv_width = key.shape[2]

    own_kv = jnp.concatenate([key[0], value[0]], axis=-1)
    kv_all = gather_ctx(own_kv, n_ctx)
    key_rows = kv_all[:, :kv_width].reshape(n_ctx * BLK, HK, HD)
    value_rows = kv_all[:, kv_width:].reshape(n_ctx * BLK, HK, HD)

    block_ids = block_lists[0, 0]
    numbers = lax.iota(jnp.int32, n_ctx)
    chosen = jnp.any(block_ids[None, :] == numbers[:, None], axis=1)
    inner = lax.iota(jnp.int32, BLK)
    causal = inner[None, :] <= inner[:, None]
    allowed = jnp.where(
        (numbers == ctx_rank)[:, None, None], causal[None], chosen[:, None, None]
    )
    allowed = jnp.transpose(allowed, (1, 0, 2)).reshape(BLK, n_ctx * BLK)

    weight_full = gather_dp(out_weight, "dp", n_dp)

    queries = query[0].reshape(BLK, HK, groups, HD)
    raw = jnp.einsum("tkgd,ukd->kgtu", queries, key_rows, preferred_element_type=jnp.float32)
    logits = jnp.where(allowed, raw * SCALE, NEGATIVE)
    row_max = jnp.max(logits, axis=-1)
    exp_total = jnp.sum(jnp.where(allowed, jnp.exp(logits - row_max[..., None]), 0.0), axis=-1)
    log_total = row_max + jnp.log(exp_total)
    attn_probs = jnp.where(allowed, jnp.exp(logits - log_total[..., None]), 0.0)
    probs_low = attn_probs.astype(jnp.bfloat16)
    heads_out = jnp.einsum(
        "kgtu,ukd->tkgd", probs_low, value_rows, preferred_element_type=jnp.float32
    ).astype(jnp.bfloat16)
    heads_flat = heads_out.reshape(tokens, HQ * HD)

    order = w_order(n_dp)
    back_order = [order.index(b) for b in range(n_dp)]
    heads_w = heads_flat.reshape(tokens, n_dp, -1)[:, jnp.array(order, jnp.int32), :]
    mixed_out = jnp.dot(
        heads_w.reshape(tokens, -1), weight_full, preferred_element_type=jnp.float32
    )
    inv_rms = lax.rsqrt(jnp.mean(mixed_out * mixed_out, axis=-1, keepdims=True) + EPSILON)
    upstream = grad_out[0].astype(jnp.float32)
    scaled = upstream * post_gain
    gain_term = jnp.sum(upstream * mixed_out * inv_rms, axis=0)
    grad_mixed = (
        inv_rms
        * (
            scaled
            - mixed_out * inv_rms * inv_rms * jnp.mean(scaled * mixed_out, axis=-1, keepdims=True)
        )
    ).astype(jnp.bfloat16)

    blocks_of_heads = heads_flat.reshape(tokens, n_dp, -1)
    heads_in_order = blocks_of_heads[:, jnp.array(wo_order(n_dp), jnp.int32), :]
    wo_term = lax.dot_general(
        heads_in_order.reshape(tokens, -1),
        grad_mixed,
        (((0,), (0,)), ((), ())),
        preferred_element_type=jnp.float32,
    )
    wo_block, gain_dp = reduce_scatter_dp(wo_term, gain_term, "dp", n_dp)
    sums = all_reduce_ctx(jnp.concatenate([wo_block, gain_dp[None]], axis=0), n_dp, n_ctx)
    wo_sum = sums[:-1]
    gain_sum = sums[-1]

    grad_heads_w = lax.dot_general(
        grad_mixed, weight_full, (((1,), (1,)), ((), ())), preferred_element_type=jnp.float32
    ).astype(jnp.bfloat16)
    grad_heads = grad_heads_w.reshape(tokens, n_dp, -1)[:, jnp.array(back_order, jnp.int32), :]
    grad_float = grad_heads.reshape(BLK, HK, groups, HD)
    delta = jnp.einsum(
        "tkgd,tkgd->kgt", grad_float, heads_out, preferred_element_type=jnp.float32
    )
    grad_probs = jnp.einsum(
        "tkgd,ukd->kgtu", grad_float, value_rows, preferred_element_type=jnp.float32
    )
    grad_logits = jnp.where(
        allowed, attn_probs * (grad_probs - delta[..., None]) * SCALE, 0.0
    ).astype(jnp.bfloat16)
    grad_query = jnp.einsum(
        "kgtu,ukd->tkgd", grad_logits, key_rows, preferred_element_type=jnp.float32
    ).astype(jnp.bfloat16)
    key_part = jnp.einsum(
        "kgtu,tkgd->ukd", grad_logits, queries, preferred_element_type=jnp.float32
    )
    value_part = jnp.einsum(
        "kgtu,tkgd->ukd", probs_low, grad_float, preferred_element_type=jnp.float32
    )
    kv_grad = jnp.concatenate(
        [key_part.reshape(n_ctx, BLK, kv_width), value_part.reshape(n_ctx, BLK, kv_width)],
        axis=-1,
    )
    total = lax.dynamic_index_in_dim(kv_grad, ctx_rank, axis=0, keepdims=False)
    for s in range(1, n_ctx):
        part = lax.dynamic_index_in_dim(
            kv_grad, jnp.maximum(ctx_rank - s, 0), axis=0, keepdims=False
        )
        back = lax.ppermute(part.astype(jnp.bfloat16), "ctx", [(i, i - s) for i in range(s, n_ctx)])
        total = total + back.astype(jnp.float32)

    seq_count = float(n_dp)
    grad_query_out = grad_query.reshape(1, tokens, HQ * HD)
    grad_key_out = total[:, :kv_width].astype(jnp.bfloat16).reshape(1, tokens, kv_width)
    grad_value_out = total[:, kv_width:].astype(jnp.bfloat16).reshape(1, tokens, kv_width)
    return (grad_query_out, grad_key_out, grad_value_out, wo_sum / seq_count, gain_sum / seq_count)


def solution(mesh):
    in_specs = (
        P("dp", "ctx", None),
        P("dp", "ctx", None),
        P("dp", "ctx", None),
        P("dp", None),
        P(),
        P("dp", "ctx", None),
        P("dp", "ctx", None),
    )
    out_specs = (
        P("dp", "ctx", None),
        P("dp", "ctx", None),
        P("dp", "ctx", None),
        P("dp", None),
        P(),
    )

    return jax.shard_map(
        per_device, mesh=mesh, in_specs=in_specs, out_specs=out_specs, check_vma=False
    )
```

```python
import jax
import jax.numpy as jnp
from jax import lax
from jax.sharding import PartitionSpec as P


HD = 256
HQ = 4
HK = 2
BLK = 128


SCALE = 0.0625
NEGATIVE = -1e30
EPSILON = 1e-06


def xor_pairs(size, mask0, mask1=None):
    mask1 = mask0 if mask1 is None else mask1
    return [(i, i ^ (mask0 if i % 2 == 0 else mask1)) for i in range(size)]


def bit_of(axis, mask):
    return (lax.axis_index(axis) // mask) % 2


def core_bit(axis):
    return lax.axis_index(axis) % 2


def z_shift(size):
    return 2 if size // 4 >= 4 else 0


def dp_label(index, size):
    if index % 2 == 0:
        return index
    z, rest = divmod(index, 4)
    return ((z + z_shift(size)) % (size // 4)) * 4 + rest


def dp_unlabel(label, size):
    if label % 2 == 0:
        return label
    z, rest = divmod(label, 4)
    return ((z - z_shift(size)) % (size // 4)) * 4 + rest


def dp_pairs(size, mask0, mask1):
    if mask0 == 1:
        return [(i, i ^ 1) for i in range(size)]
    pairs = []
    for i in range(size):
        mask = mask0 if i % 2 == 0 else mask1
        pairs.append((i, dp_unlabel(dp_label(i, size) ^ mask, size)))
    return pairs


def own_bit(axis, size, mask0, mask1):
    index = lax.axis_index(axis)
    if mask0 != 1:
        shifted = ((index // 4 + z_shift(size)) % (size // 4)) * 4 + index % 4
        index = jnp.where(index % 2 == 1, shifted, index)
    mask = jnp.where(core_bit(axis) == 0, mask0, mask1)
    return (index // mask) % 2


def roll_z(held, size, amount):
    lead = held.ndim - 2 - 1
    shape = held.shape
    zs = size // 4
    grouped = held.reshape((zs,) + shape[lead:])
    return jnp.roll(grouped, amount, axis=0).reshape(shape)


def split_rounds(size):
    bits = size.bit_length() - 1
    high = [1 << k for k in range(3, bits)]
    return [(1, 1), (4, 2), (2, 4)] + [(m, m) for m in high]


def gather_dp(block, axis, size):
    rounds = split_rounds(size)[::-1]
    held = block
    count = 0
    for mask0, mask1 in rounds:
        if mask0 == 1:
            held = jnp.where(
                core_bit(axis) == 0,
                jnp.swapaxes(held, count - 2, count - 1),
                roll_z(held, size, -z_shift(size)),
            )
        theirs = lax.ppermute(held, axis, dp_pairs(size, mask0, mask1))
        mine_high = own_bit(axis, size, mask0, mask1) == 1
        low = jnp.where(mine_high, theirs, held)
        high = jnp.where(mine_high, held, theirs)
        held = jnp.stack([low, high], axis=count)
        count += 1
    return held.reshape((size * block.shape[0],) + block.shape[1:])


def wo_order(size):
    order = []
    for q in range(size):
        if q % 2 == 0:
            order.append(q)
            continue
        high, x_hi, z_low = q >> 3, (q >> 2) & 1, (q >> 1) & 1
        z = (high * 2 + z_low - z_shift(size)) % (size // 4)
        order.append(z * 4 + x_hi * 2 + 1)
    return order


def split_hi_lo(value):
    hi = value.astype(jnp.bfloat16)
    lo = (value - hi.astype(jnp.float32)).astype(jnp.bfloat16)
    return hi, lo


def reduce_scatter_dp(full, gain, axis, size):
    bits = size.bit_length() - 1
    rows = full.shape[0] // size
    cols = full.shape[1]
    held = full.reshape((2,) * bits + (rows, cols))
    for mask0, mask1 in split_rounds(size):
      pos = held.ndim - 3
      if mask0 == 4:
          pos = pos - 1
      mine = own_bit(axis, size, mask0, mask1)
      keep = lax.dynamic_index_in_dim(held, mine, axis=pos, keepdims=False)
      send = lax.dynamic_index_in_dim(held, 1 - mine, axis=pos, keepdims=False)
      hi, lo = split_hi_lo(gain)
      packet = jnp.concatenate(
          [send.astype(jnp.bfloat16).reshape(-1, cols), hi[None], lo[None]], axis=0
      )
      theirs = lax.ppermute(packet, axis, dp_pairs(size, mask0, mask1))
      got = theirs[:-2].reshape(send.shape).astype(jnp.float32)
      held = keep.astype(jnp.float32) + got
      mine_gain = hi.astype(jnp.float32) + lo.astype(jnp.float32)
      their_gain = theirs[-2].astype(jnp.float32) + theirs[-1].astype(jnp.float32)
      gain = mine_gain + their_gain
    return held.reshape(rows, cols), gain


def all_reduce_ctx(value, n_dp, n_ctx):
    bits = n_ctx.bit_length() - 1
    order0 = [1 << k for k in range(bits)]
    order1 = order0[-1:] + order0[:-1]
    for mask0, mask1 in zip(order0, order1):
        perm = []
        for d in range(n_dp):
            mask = mask0 if d % 2 == 0 else mask1
            perm += [(d * n_ctx + c, d * n_ctx + (c ^ mask)) for c in range(n_ctx)]
        value = value + lax.ppermute(value, ("dp", "ctx"), perm)
    return value


def gather_ctx(block, size):
    held = block
    done = []
    for mask in (2, 1, 4):
        if mask >= size:
            continue
        theirs = lax.ppermute(held, "ctx", xor_pairs(size, mask))
        mine_high = bit_of("ctx", mask) == 1
        low = jnp.where(mine_high, theirs, held)
        high = jnp.where(mine_high, held, theirs)
        pos = sum(1 for m in done if m > mask)
        held = jnp.stack([low, high], axis=pos)
        done.append(mask)
    return held.reshape((size * block.shape[0],) + block.shape[1:])


def per_device(query, key, value, out_weight, post_gain, grad_out, block_lists):
    tokens = query.shape[1]
    assert tokens == BLK
    groups = HQ // HK
    n_ctx = lax.axis_size("ctx")
    n_dp = lax.axis_size("dp")
    ctx_rank = lax.axis_index("ctx")
    kv_width = key.shape[2]

    own_kv = jnp.concatenate([key[0], value[0]], axis=-1)
    kv_all = gather_ctx(own_kv, n_ctx)
    key_rows = kv_all[:, :kv_width].reshape(n_ctx * BLK, HK, HD)
    value_rows = kv_all[:, kv_width:].reshape(n_ctx * BLK, HK, HD)

    block_ids = block_lists[0, 0]
    numbers = lax.iota(jnp.int32, n_ctx)
    chosen = jnp.any(block_ids[None, :] == numbers[:, None], axis=1)
    inner = lax.iota(jnp.int32, BLK)
    causal = inner[None, :] <= inner[:, None]
    allowed = jnp.where(
        (numbers == ctx_rank)[:, None, None], causal[None], chosen[:, None, None]
    )
    allowed = jnp.transpose(allowed, (1, 0, 2)).reshape(BLK, n_ctx * BLK)

    weight_full = gather_dp(out_weight, "dp", n_dp)

    queries = query[0].reshape(BLK, HK, groups, HD)
    raw = jnp.einsum("tkgd,ukd->kgtu", queries, key_rows, preferred_element_type=jnp.float32)
    logits = jnp.where(allowed, raw * SCALE, NEGATIVE)
    row_max = jnp.max(logits, axis=-1)
    exp_total = jnp.sum(jnp.where(allowed, jnp.exp(logits - row_max[..., None]), 0.0), axis=-1)
    log_total = row_max + jnp.log(exp_total)
    attn_probs = jnp.where(allowed, jnp.exp(logits - log_total[..., None]), 0.0)
    probs_low = attn_probs.astype(jnp.bfloat16)
    heads_out = jnp.einsum(
        "kgtu,ukd->tkgd", probs_low, value_rows, preferred_element_type=jnp.float32
    ).astype(jnp.bfloat16)
    heads_flat = heads_out.reshape(tokens, HQ * HD)

    mixed_out = jnp.dot(heads_flat, weight_full, preferred_element_type=jnp.float32)
    inv_rms = lax.rsqrt(jnp.mean(mixed_out * mixed_out, axis=-1, keepdims=True) + EPSILON)
    upstream = grad_out[0].astype(jnp.float32)
    scaled = upstream * post_gain
    gain_term = jnp.sum(upstream * mixed_out * inv_rms, axis=0)
    grad_mixed = (
        inv_rms
        * (
            scaled
            - mixed_out * inv_rms * inv_rms * jnp.mean(scaled * mixed_out, axis=-1, keepdims=True)
        )
    ).astype(jnp.bfloat16)

    blocks_of_heads = heads_flat.reshape(tokens, n_dp, -1)
    heads_in_order = blocks_of_heads[:, jnp.array(wo_order(n_dp), jnp.int32), :]
    wo_term = lax.dot_general(
        heads_in_order.reshape(tokens, -1),
        grad_mixed,
        (((0,), (0,)), ((), ())),
        preferred_element_type=jnp.float32,
    )
    half = wo_term.shape[1] // 2
    gain_halves = (gain_term[:half], gain_term[half:])
    wo_parts, gain_parts = [], []
    for k in range(2):
        block_k, gain_k = reduce_scatter_dp(
            wo_term[:, k * half:(k + 1) * half], gain_halves[k], "dp", n_dp
        )
        sums_k = all_reduce_ctx(jnp.concatenate([block_k, gain_k[None]], axis=0), n_dp, n_ctx)
        wo_parts.append(sums_k[:-1])
        gain_parts.append(sums_k[-1])
    wo_sum = jnp.concatenate(wo_parts, axis=1)
    gain_sum = jnp.concatenate(gain_parts)

    grad_heads = lax.dot_general(
        grad_mixed, weight_full, (((1,), (1,)), ((), ())), preferred_element_type=jnp.float32
    ).astype(jnp.bfloat16)
    grad_float = grad_heads.reshape(BLK, HK, groups, HD)
    delta = jnp.einsum(
        "tkgd,tkgd->kgt", grad_float, heads_out, preferred_element_type=jnp.float32
    )
    grad_probs = jnp.einsum(
        "tkgd,ukd->kgtu", grad_float, value_rows, preferred_element_type=jnp.float32
    )
    grad_logits = jnp.where(
        allowed, attn_probs * (grad_probs - delta[..., None]) * SCALE, 0.0
    ).astype(jnp.bfloat16)
    grad_query = jnp.einsum(
        "kgtu,ukd->tkgd", grad_logits, key_rows, preferred_element_type=jnp.float32
    ).astype(jnp.bfloat16)
    key_part = jnp.einsum(
        "kgtu,tkgd->ukd", grad_logits, queries, preferred_element_type=jnp.float32
    )
    value_part = jnp.einsum(
        "kgtu,tkgd->ukd", probs_low, grad_float, preferred_element_type=jnp.float32
    )
    kv_grad = jnp.concatenate(
        [key_part.reshape(n_ctx, BLK, kv_width), value_part.reshape(n_ctx, BLK, kv_width)],
        axis=-1,
    )
    total = lax.dynamic_index_in_dim(kv_grad, ctx_rank, axis=0, keepdims=False)
    for s in range(1, n_ctx):
        part = lax.dynamic_index_in_dim(
            kv_grad, jnp.maximum(ctx_rank - s, 0), axis=0, keepdims=False
        )
        back = lax.ppermute(part.astype(jnp.bfloat16), "ctx", [(i, i - s) for i in range(s, n_ctx)])
        total = total + back.astype(jnp.float32)

    seq_count = float(n_dp)
    grad_query_out = grad_query.reshape(1, tokens, HQ * HD)
    grad_key_out = total[:, :kv_width].astype(jnp.bfloat16).reshape(1, tokens, kv_width)
    grad_value_out = total[:, kv_width:].astype(jnp.bfloat16).reshape(1, tokens, kv_width)
    return (grad_query_out, grad_key_out, grad_value_out, wo_sum / seq_count, gain_sum / seq_count)


def solution(mesh):
    in_specs = (
        P("dp", "ctx", None),
        P("dp", "ctx", None),
        P("dp", "ctx", None),
        P("dp", None),
        P(),
        P("dp", "ctx", None),
        P("dp", "ctx", None),
    )
    out_specs = (
        P("dp", "ctx", None),
        P("dp", "ctx", None),
        P("dp", "ctx", None),
        P("dp", None),
        P(),
    )

    return jax.shard_map(
        per_device, mesh=mesh, in_specs=in_specs, out_specs=out_specs, check_vma=False
    )
```

```python
import jax
import jax.numpy as jnp
from jax import lax
from jax.sharding import PartitionSpec as P


HD = 256
HQ = 4
HK = 2
BLK = 128


SCALE = 0.0625
NEGATIVE = -1e30
EPSILON = 1e-06


def xor_pairs(size, mask0, mask1=None):
    mask1 = mask0 if mask1 is None else mask1
    return [(i, i ^ (mask0 if i % 2 == 0 else mask1)) for i in range(size)]


def bit_of(axis, mask):
    return (lax.axis_index(axis) // mask) % 2


def core_bit(axis):
    return lax.axis_index(axis) % 2


def z_shift(size):
    return 2 if size // 4 >= 4 else 0


def dp_label(index, size):
    if index % 2 == 0:
        return index
    z, rest = divmod(index, 4)
    return ((z + z_shift(size)) % (size // 4)) * 4 + rest


def dp_unlabel(label, size):
    if label % 2 == 0:
        return label
    z, rest = divmod(label, 4)
    return ((z - z_shift(size)) % (size // 4)) * 4 + rest


def dp_pairs(size, mask0, mask1):
    if mask0 == 1:
        return [(i, i ^ 1) for i in range(size)]
    pairs = []
    for i in range(size):
        mask = mask0 if i % 2 == 0 else mask1
        pairs.append((i, dp_unlabel(dp_label(i, size) ^ mask, size)))
    return pairs


def own_bit(axis, size, mask0, mask1):
    index = lax.axis_index(axis)
    if mask0 != 1:
        shifted = ((index // 4 + z_shift(size)) % (size // 4)) * 4 + index % 4
        index = jnp.where(index % 2 == 1, shifted, index)
    mask = jnp.where(core_bit(axis) == 0, mask0, mask1)
    return (index // mask) % 2


def roll_z(held, size, amount):
    lead = held.ndim - 2 - 1
    shape = held.shape
    zs = size // 4
    grouped = held.reshape((zs,) + shape[lead:])
    return jnp.roll(grouped, amount, axis=0).reshape(shape)


def split_rounds(size):
    bits = size.bit_length() - 1
    high = [1 << k for k in range(3, bits)]
    return [(1, 1), (4, 2), (2, 4)] + [(m, m) for m in high]


def gather_dp(block, axis, size):
    rounds = split_rounds(size)[::-1]
    held = block
    count = 0
    for mask0, mask1 in rounds:
        if mask0 == 1:
            held = jnp.where(
                core_bit(axis) == 0,
                jnp.swapaxes(held, count - 2, count - 1),
                roll_z(held, size, -z_shift(size)),
            )
        theirs = lax.ppermute(held, axis, dp_pairs(size, mask0, mask1))
        mine_high = own_bit(axis, size, mask0, mask1) == 1
        low = jnp.where(mine_high, theirs, held)
        high = jnp.where(mine_high, held, theirs)
        held = jnp.stack([low, high], axis=count)
        count += 1
    return held.reshape((size * block.shape[0],) + block.shape[1:])


def wo_order(size):
    order = []
    for q in range(size):
        if q % 2 == 0:
            order.append(q)
            continue
        high, x_hi, z_low = q >> 3, (q >> 2) & 1, (q >> 1) & 1
        z = (high * 2 + z_low - z_shift(size)) % (size // 4)
        order.append(z * 4 + x_hi * 2 + 1)
    return order


def split_hi_lo(value):
    hi = value.astype(jnp.bfloat16)
    lo = (value - hi.astype(jnp.float32)).astype(jnp.bfloat16)
    return hi, lo


def reduce_scatter_dp(full, gain, axis, size):
    bits = size.bit_length() - 1
    rows = full.shape[0] // size
    cols = full.shape[1]
    held = full.reshape((2,) * bits + (rows, cols))
    for mask0, mask1 in split_rounds(size):
      pos = held.ndim - 3
      if mask0 == 4:
          pos = pos - 1
      mine = own_bit(axis, size, mask0, mask1)
      keep = lax.dynamic_index_in_dim(held, mine, axis=pos, keepdims=False)
      send = lax.dynamic_index_in_dim(held, 1 - mine, axis=pos, keepdims=False)
      hi, lo = split_hi_lo(gain)
      packet = jnp.concatenate(
          [send.astype(jnp.bfloat16).reshape(-1, cols), hi[None], lo[None]], axis=0
      )
      theirs = lax.ppermute(packet, axis, dp_pairs(size, mask0, mask1))
      got = theirs[:-2].reshape(send.shape).astype(jnp.float32)
      held = keep.astype(jnp.float32) + got
      mine_gain = hi.astype(jnp.float32) + lo.astype(jnp.float32)
      their_gain = theirs[-2].astype(jnp.float32) + theirs[-1].astype(jnp.float32)
      gain = mine_gain + their_gain
    return held.reshape(rows, cols), gain


def all_reduce_ctx(value, n_dp, n_ctx):
    bits = n_ctx.bit_length() - 1
    order0 = [1 << k for k in range(bits)]
    order1 = order0[-1:] + order0[:-1]
    for mask0, mask1 in zip(order0, order1):
        perm = []
        for d in range(n_dp):
            mask = mask0 if d % 2 == 0 else mask1
            perm += [(d * n_ctx + c, d * n_ctx + (c ^ mask)) for c in range(n_ctx)]
        value = value + lax.ppermute(value, ("dp", "ctx"), perm)
    return value


def gather_ctx(block, size):
    held = block
    done = []
    for mask in (2, 1, 4):
        if mask >= size:
            continue
        theirs = lax.ppermute(held, "ctx", xor_pairs(size, mask))
        mine_high = bit_of("ctx", mask) == 1
        low = jnp.where(mine_high, theirs, held)
        high = jnp.where(mine_high, held, theirs)
        pos = sum(1 for m in done if m > mask)
        held = jnp.stack([low, high], axis=pos)
        done.append(mask)
    return held.reshape((size * block.shape[0],) + block.shape[1:])


def per_device(query, key, value, out_weight, post_gain, grad_out, block_lists):
    tokens = query.shape[1]
    assert tokens == BLK
    groups = HQ // HK
    n_ctx = lax.axis_size("ctx")
    n_dp = lax.axis_size("dp")
    ctx_rank = lax.axis_index("ctx")
    kv_width = key.shape[2]

    own_kv = jnp.concatenate([key[0], value[0]], axis=-1)
    kv_all = gather_ctx(own_kv, n_ctx)
    key_rows = kv_all[:, :kv_width].reshape(n_ctx * BLK, HK, HD)
    value_rows = kv_all[:, kv_width:].reshape(n_ctx * BLK, HK, HD)

    block_ids = block_lists[0, 0]
    numbers = lax.iota(jnp.int32, n_ctx)
    chosen = jnp.any(block_ids[None, :] == numbers[:, None], axis=1)
    inner = lax.iota(jnp.int32, BLK)
    causal = inner[None, :] <= inner[:, None]
    allowed = jnp.where(
        (numbers == ctx_rank)[:, None, None], causal[None], chosen[:, None, None]
    )
    allowed = jnp.transpose(allowed, (1, 0, 2)).reshape(BLK, n_ctx * BLK)

    weight_full = gather_dp(out_weight, "dp", n_dp)

    queries = query[0].reshape(BLK, HK, groups, HD)
    raw = jnp.einsum("tkgd,ukd->kgtu", queries, key_rows, preferred_element_type=jnp.float32)
    logits = jnp.where(allowed, raw * SCALE, NEGATIVE)
    row_max = jnp.max(logits, axis=-1)
    exp_total = jnp.sum(jnp.where(allowed, jnp.exp(logits - row_max[..., None]), 0.0), axis=-1)
    log_total = row_max + jnp.log(exp_total)
    attn_probs = jnp.where(allowed, jnp.exp(logits - log_total[..., None]), 0.0)
    probs_low = attn_probs.astype(jnp.bfloat16)
    heads_out = jnp.einsum(
        "kgtu,ukd->tkgd", probs_low, value_rows, preferred_element_type=jnp.float32
    ).astype(jnp.bfloat16)
    heads_flat = heads_out.reshape(tokens, HQ * HD)

    mixed_out = jnp.dot(heads_flat, weight_full, preferred_element_type=jnp.float32)
    inv_rms = lax.rsqrt(jnp.mean(mixed_out * mixed_out, axis=-1, keepdims=True) + EPSILON)
    upstream = grad_out[0].astype(jnp.float32)
    scaled = upstream * post_gain
    gain_term = jnp.sum(upstream * mixed_out * inv_rms, axis=0)
    grad_mixed = (
        inv_rms
        * (
            scaled
            - mixed_out * inv_rms * inv_rms * jnp.mean(scaled * mixed_out, axis=-1, keepdims=True)
        )
    ).astype(jnp.bfloat16)

    blocks_of_heads = heads_flat.reshape(tokens, n_dp, -1)
    heads_in_order = blocks_of_heads[:, jnp.array(wo_order(n_dp), jnp.int32), :]
    wo_term = lax.dot_general(
        heads_in_order.reshape(tokens, -1),
        grad_mixed,
        (((0,), (0,)), ((), ())),
        preferred_element_type=jnp.float32,
    )
    wo_block, gain_dp = reduce_scatter_dp(wo_term, gain_term, "dp", n_dp)
    sums = all_reduce_ctx(jnp.concatenate([wo_block, gain_dp[None]], axis=0), n_dp, n_ctx)
    wo_sum = sums[:-1]
    gain_sum = sums[-1]

    grad_heads = lax.dot_general(
        grad_mixed, weight_full, (((1,), (1,)), ((), ())), preferred_element_type=jnp.float32
    ).astype(jnp.bfloat16)
    grad_float = grad_heads.reshape(BLK, HK, groups, HD)
    delta = jnp.einsum(
        "tkgd,tkgd->kgt", grad_float, heads_out, preferred_element_type=jnp.float32
    )
    grad_probs = jnp.einsum(
        "tkgd,ukd->kgtu", grad_float, value_rows, preferred_element_type=jnp.float32
    )
    grad_logits = jnp.where(
        allowed, attn_probs * (grad_probs - delta[..., None]) * SCALE, 0.0
    ).astype(jnp.bfloat16)
    grad_query = jnp.einsum(
        "kgtu,ukd->tkgd", grad_logits, key_rows, preferred_element_type=jnp.float32
    ).astype(jnp.bfloat16)
    key_part = jnp.einsum(
        "kgtu,tkgd->ukd", grad_logits, queries, preferred_element_type=jnp.float32
    )
    value_part = jnp.einsum(
        "kgtu,tkgd->ukd", probs_low, grad_float, preferred_element_type=jnp.float32
    )
    kv_grad = jnp.concatenate(
        [key_part.reshape(n_ctx, BLK, kv_width), value_part.reshape(n_ctx, BLK, kv_width)],
        axis=-1,
    )
    total = lax.dynamic_index_in_dim(kv_grad, ctx_rank, axis=0, keepdims=False)
    for s in range(1, n_ctx):
        part = lax.dynamic_index_in_dim(
            kv_grad, jnp.maximum(ctx_rank - s, 0), axis=0, keepdims=False
        )
        back = lax.ppermute(part.astype(jnp.bfloat16), "ctx", [(i, i - s) for i in range(s, n_ctx)])
        total = total + back.astype(jnp.float32)

    seq_count = float(n_dp)
    grad_query_out = grad_query.reshape(1, tokens, HQ * HD)
    grad_key_out = total[:, :kv_width].astype(jnp.bfloat16).reshape(1, tokens, kv_width)
    grad_value_out = total[:, kv_width:].astype(jnp.bfloat16).reshape(1, tokens, kv_width)
    return (grad_query_out, grad_key_out, grad_value_out, wo_sum / seq_count, gain_sum / seq_count)


def solution(mesh):
    in_specs = (
        P("dp", "ctx", None),
        P("dp", "ctx", None),
        P("dp", "ctx", None),
        P("dp", None),
        P(),
        P("dp", "ctx", None),
        P("dp", "ctx", None),
    )
    out_specs = (
        P("dp", "ctx", None),
        P("dp", "ctx", None),
        P("dp", "ctx", None),
        P("dp", None),
        P(),
    )

    return jax.shard_map(
        per_device, mesh=mesh, in_specs=in_specs, out_specs=out_specs, check_vma=False
    )
```
